512 devices in a mesh: col: 8 (over z), tile: 64 (over y, x, core).
Axes of the slice: x: 4, y: 8, z: 8, core: 2. Of those that a mesh axis runs over, the one named last changes fastest.
Arguments:
- panel_factor: bfloat16 [8, 64, 2, 512, 512], P('col', 'tile'), may hold values from -0.15625 to 0.15625
- panel_cotangent: bfloat16 [8, 64, 2, 512, 512], P('col', 'tile'), may hold values from -1.5 to 1.5
- diag_factor: bfloat16 [8, 512, 512], P('col'), as said below
- diag_inverse: bfloat16 [8, 512, 512], P('col'), as said below
- diag_cotangent: float32 [8, 512, 512], P('col', 'tile'), may hold values from -6 to 6
- tile_count: int32 [8, 64], P('col', 'tile'), may hold values from 1 to 2, as said below
- tile_rows: int32 [8, 64, 2], P('col', 'tile'), may hold values from 1 to 255, as said below
Outputs:
- panel_adjoint: bfloat16 [8, 64, 2, 512, 512], P('col', 'tile')
- diag_adjoint: float32 [8, 512, 512], P('col', 'tile')
The draws below stay inside these ranges and needn't reach their ends.
Inputs may be any that keep to these rules, and one draw needn't show every extreme that they name: `tile_count`: every device holds 1 to 2 live tiles of each panel column, in its first slots; in every column some device holds 2. `tile_rows`: in column c the live slots name distinct block rows; exactly one live slot names row c + 1, every other slot names a row of c + 2 or more. `diag_factor`: lower triangular with diagonal entries between 0.8 and 1.6. `diag_inverse`: lower triangular with diagonal entries between 0.8 and 1.6.
All inputs are finite; a program needn't handle non-finite values.
Results may differ from the reference program's by a relative error of at most 0.0044.
Values sent between devices are 32-bit elements; how exact they have to be, the bound alone decides.
No kernel may reach another device: no remote copies, remote signals or barrier semaphores. Data moves between devices by JAX's collectives and lax.ppermute only.
A program may use at most 128 MiB of HBM per device.

```python
import jax
import jax.numpy as jnp
from jax import lax

B = 512
SLOTS = 2
BLOCK_ROWS = 256
N_COLS = 8
N_TILE = 64


def lower_triangle(key):
    first, second = jax.random.split(key)
    spread = jax.random.normal(first, (N_COLS, B, B), jnp.float32)
    spread = spread * B ** (-0.5)
    diagonal = jax.random.uniform(second, (N_COLS, B), jnp.float32, 0.8, 1.6)
    row_index = jnp.arange(B)[:, None]
    col_index = jnp.arange(B)[None, :]
    strict = jnp.where(row_index > col_index, spread, 0.0)
    diag_part = jnp.where(row_index == col_index, diagonal[:, :, None], 0.0)
    return (strict + diag_part).astype(jnp.bfloat16)


def draw_diag_factor(key, part):
    return lower_triangle(jax.random.fold_in(key, 11))


def draw_diag_inverse(key, part):
    return lower_triangle(jax.random.fold_in(key, 12))


def draw_tile_count(key, part):
    first = jax.random.fold_in(key, 21)
    second = jax.random.fold_in(key, 22)
    counts = jax.random.randint(first, (N_COLS, N_TILE), 1, SLOTS + 1, jnp.int32)
    busiest = jax.random.randint(second, (N_COLS,), 0, N_TILE, jnp.int32)
    place = jnp.arange(N_TILE, dtype=jnp.int32)[None, :]
    return jnp.where(place == busiest[:, None], SLOTS, counts).astype(jnp.int32)


def draw_tile_rows(key, part):
    columns = []
    for column in range(N_COLS):
        column_key = jax.random.fold_in(jax.random.fold_in(key, 31), column)
        shuffled = jax.random.permutation(column_key, BLOCK_ROWS - N_COLS - 1).astype(jnp.int32)
        picked = shuffled[:N_TILE * SLOTS] + column + 2
        picked = picked.reshape(N_TILE, SLOTS)
        owner = jax.random.randint(jax.random.fold_in(column_key, 99), (), 0, N_TILE, jnp.int32)
        place = jnp.arange(N_TILE, dtype=jnp.int32)[:, None]
        first_slot = jnp.arange(SLOTS, dtype=jnp.int32)[None, :] == 0
        picked = jnp.where((place == owner) & first_slot, column + 1, picked)
        columns.append(picked.astype(jnp.int32))
    return jnp.stack(columns, axis=0)


def shard_levels(stream_key, shape, cuts, smallest, high):
    def one(position, shards_of):
        heights = jax.random.uniform(jax.random.fold_in(jax.random.fold_in(stream_key, 6), position), (shards_of,), jnp.float32, smallest / len(cuts), high / len(cuts))
        return jnp.repeat(jnp.exp(heights), shape[position] // shards_of).reshape((-1,) + (1,) * (len(shape) - position - 1))

    gain = one(*cuts[0])
    for cut in cuts[1:]:
        gain = gain * one(*cut)
    return gain


def scatter_about(rng, shape, scale, limit, cuts=(), kind=jnp.bfloat16):
    drawn = jax.random.normal(rng, shape, jnp.float32) * scale
    if len(cuts) > 0:
        drawn = shard_levels(rng, shape, cuts, -0.22, 0.18) * drawn
    return jnp.clip(drawn, min=-limit, max=limit).astype(kind)


def setup_inputs(seed: int = 0) -> dict:
    seeds = jax.random.split(jax.random.key(seed), 8)
    panel_factor = scatter_about(seeds[0], (N_COLS, N_TILE, SLOTS, B, B), (3 * B) ** -0.5, 0.15625, ((0, 8), (1, 64)))
    panel_cotangent = scatter_about(seeds[1], (N_COLS, N_TILE, SLOTS, B, B), 0.25, 1.5, ((0, 8), (1, 64)))
    diag_factor = draw_diag_factor(jax.random.fold_in(seeds[7], 71), 0)
    diag_inverse = draw_diag_inverse(jax.random.fold_in(seeds[7], 71), 0)
    diag_cotangent = scatter_about(seeds[4], (N_COLS, B, B), 1.0, 6.0, ((0, 8), (1, 64)), jnp.float32)
    tile_count = draw_tile_count(jax.random.fold_in(seeds[7], 71), 0)
    tile_rows = draw_tile_rows(jax.random.fold_in(seeds[7], 71), 0)
    return {"panel_factor": panel_factor, "panel_cotangent": panel_cotangent, "diag_factor": diag_factor, "diag_inverse": diag_inverse, "diag_cotangent": diag_cotangent, "tile_count": tile_count, "tile_rows": tile_rows}


def symmetrize(matrix):
    strict = jnp.tril(matrix, -1)
    return strict + strict.T + jnp.diag(jnp.diagonal(matrix))


def reference(panel_factor, panel_cotangent, diag_factor, diag_inverse, diag_cotangent, tile_count, tile_rows):
    full = lax.Precision.HIGHEST
    later = jnp.zeros((B, B), jnp.float32)
    adjoints = []
    panels = []
    for column in range(N_COLS - 1, -1, -1):
        factors = panel_factor[column]
        inverse = diag_inverse[column]
        live_slot = jnp.arange(SLOTS)[None, :] < tile_count[column][:, None]
        link_flag = live_slot & (tile_rows[column] == column + 1)
        solved = jnp.einsum("tsij,jk->tsik", panel_cotangent[column].astype(jnp.float32), inverse.astype(jnp.float32))
        rounded = jnp.where(live_slot[:, :, None, None], solved.astype(jnp.bfloat16), jnp.zeros_like(solved, dtype=jnp.bfloat16))
        summed = diag_cotangent[column] - jnp.einsum("tsij,tsik->jk", rounded.astype(jnp.float32), factors.astype(jnp.float32))
        chosen = jnp.sum(jnp.where(link_flag[:, :, None, None], factors.astype(jnp.float32), 0.0), axis=(0, 1))
        link_wide = jnp.dot(chosen.astype(jnp.bfloat16), inverse, preferred_element_type=jnp.float32)
        inverse_wide = inverse.astype(jnp.float32)
        curvature = jnp.dot(diag_factor[column].astype(jnp.float32).T, summed, precision=full)
        symmetric = symmetrize(curvature)
        own_map = 0.5 * jnp.dot(inverse_wide.T, jnp.dot(symmetric, inverse_wide, precision=full), precision=full)
        product = jnp.dot(later, link_wide, precision=full)
        current = own_map + jnp.dot(link_wide.T, product, precision=full)
        adjusted = (solved - 2.0 * product[None, None]).astype(jnp.bfloat16)
        panel = jnp.where(link_flag[:, :, None, None], adjusted, rounded)
        adjoints.append(current)
        panels.append(panel)
        later = current
    panel_adjoint = jnp.stack(panels[::-1], axis=0)
    diag_adjoint = jnp.stack(adjoints[::-1], axis=0)
    return panel_adjoint, diag_adjoint
```

```python
import jax
import jax.numpy as jnp
from jax import lax
from jax.sharding import PartitionSpec as P


def exchange(value, axis, count, bit):
    return lax.ppermute(value, axis, [(i, i ^ bit) for i in range(count)])


def all_sum(value, axis):
    count = lax.axis_size(axis)
    pieces = value.reshape((count, value.shape[0] // count) + value.shape[1:])
    share = jnp.sum(lax.all_to_all(pieces, axis, 0, 0), axis=0)
    spread = jnp.broadcast_to(share[None], pieces.shape)
    return lax.all_to_all(spread, axis, 0, 0).reshape(value.shape)


def passed_down(value, axis):
    count = lax.axis_size(axis)
    return lax.ppermute(value, axis, [(i, i - 1) for i in range(1, count)])


def symmetrize(matrix):
    strict = jnp.tril(matrix, -1)
    return strict + strict.T + jnp.diag(jnp.diagonal(matrix))


def on_device(
    panel_factor, panel_cotangent, diag_factor, diag_inverse, diag_cotangent, tile_count, tile_rows
):
    full = lax.Precision.HIGHEST
    factors = panel_factor[0, 0]
    cotangent = panel_cotangent[0, 0]
    lower = diag_factor[0]
    inverse = diag_inverse[0]
    width = lower.shape[0]
    rows_dev = diag_cotangent.shape[1]
    slot_count = factors.shape[0]
    column = lax.axis_index("col")
    groups = lax.axis_size("col")
    tile = lax.axis_index("tile")
    row_start = tile * rows_dev
    live_slot = jnp.arange(slot_count) < tile_count[0, 0]
    link_flag = live_slot & (tile_rows[0, 0] == column + 1)
    solved = jnp.einsum("sij,jk->sik", cotangent, inverse, preferred_element_type=jnp.float32)
    rounded = jnp.where(
        live_slot[:, None, None], solved.astype(jnp.bfloat16), jnp.zeros_like(cotangent)
    )
    panel_terms = -jnp.einsum("sij,sik->jk", rounded, factors, preferred_element_type=jnp.float32)
    own_rows = lax.dynamic_slice_in_dim(panel_terms, row_start, rows_dev, 0) + diag_cotangent[0]
    panel_terms = lax.dynamic_update_slice_in_dim(panel_terms, own_rows, row_start, 0)
    chosen = jnp.sum(jnp.where(link_flag[:, None, None], factors, jnp.zeros_like(factors)), axis=0)
    link_part = jnp.dot(chosen, inverse, preferred_element_type=jnp.float32)
    reduced = all_sum(jnp.concatenate([panel_terms, link_part], axis=0), "tile")
    summed = reduced[:width]
    link_wide = reduced[width:]
    inverse_wide = inverse.astype(jnp.float32)
    curvature = jnp.dot(lower.astype(jnp.float32).T, summed, precision=full)
    symmetric = symmetrize(curvature)
    own_map = 0.5 * jnp.dot(
        inverse_wide.T, jnp.dot(symmetric, inverse_wide, precision=full), precision=full
    )
    core = tile % 2
    half = width // 2
    incoming = jnp.zeros((width, width), jnp.float32)
    for sweep in range(groups - 1):
        advanced = own_map + jnp.dot(
            link_wide.T, jnp.dot(incoming, link_wide, precision=full), precision=full
        )
        mine = lax.dynamic_slice_in_dim(advanced, core * half, half, 0)
        arrived = passed_down(mine, "col")
        other = exchange(arrived, "tile", lax.axis_size("tile"), 1)
        whole = jnp.zeros((width, width), jnp.float32)
        whole = lax.dynamic_update_slice_in_dim(whole, arrived, core * half, 0)
        incoming = lax.dynamic_update_slice_in_dim(whole, other, (1 - core) * half, 0)
    product = jnp.dot(incoming, link_wide, precision=full)
    link_rows = lax.dynamic_slice_in_dim(link_wide, row_start, rows_dev, 1)
    own_part = lax.dynamic_slice_in_dim(own_map, row_start, rows_dev, 0)
    diag_rows = own_part + jnp.dot(link_rows.T, product, precision=full)
    adjusted = (solved - 2.0 * product[None]).astype(jnp.bfloat16)
    panel_out = jnp.where(link_flag[:, None, None], adjusted, rounded)
    return (panel_out[None, None], diag_rows[None])


def solution(mesh):
    in_specs = (
        P("col", "tile", None, None, None),
        P("col", "tile", None, None, None),
        P("col", None, None),
        P("col", None, None),
        P("col", "tile", None),
        P("col", "tile"),
        P("col", "tile", None),
    )
    out_specs = (P("col", "tile", None, None, None), P("col", "tile", None))
    return jax.shard_map(
        on_device, mesh=mesh, in_specs=in_specs, out_specs=out_specs, check_vma=False
    )
```

```python
import jax
import jax.numpy as jnp
from jax import lax
from jax.sharding import Mesh
from jax.sharding import PartitionSpec as P

TILE = ("y", "x", "core")
CHIPS = ("y", "x")


def swap_cores(value):
    return lax.ppermute(value, "core", [(0, 1), (1, 0)])


def all_sum(value):
    core = lax.axis_index("core")
    half = value.shape[0] // 2
    keep = lax.dynamic_slice_in_dim(value, core * half, half, 0)
    send = lax.dynamic_slice_in_dim(value, (1 - core) * half, half, 0)
    mine = keep + swap_cores(send)
    count = lax.axis_size(CHIPS)
    pieces = mine.reshape((count, half // count) + mine.shape[1:])
    share = jnp.sum(lax.all_to_all(pieces, CHIPS, 0, 0), axis=0)
    spread = jnp.broadcast_to(share[None], pieces.shape)
    mine = lax.all_to_all(spread, CHIPS, 0, 0).reshape(mine.shape)
    other = swap_cores(mine)
    whole = jnp.zeros(value.shape, value.dtype)
    whole = lax.dynamic_update_slice_in_dim(whole, mine, core * half, 0)
    return lax.dynamic_update_slice_in_dim(whole, other, (1 - core) * half, 0)


def symmetrize(matrix):
    rows = lax.broadcasted_iota(jnp.int32, matrix.shape, 0)
    cols = lax.broadcasted_iota(jnp.int32, matrix.shape, 1)
    return jnp.where(rows >= cols, matrix, matrix.T)


def on_device(
    panel_factor, panel_cotangent, diag_factor, diag_inverse, diag_cotangent, tile_count, tile_rows
):
    full = lax.Precision.HIGHEST
    chain = lax.Precision.HIGH
    factors = panel_factor[0, 0]
    cotangent = panel_cotangent[0, 0]
    lower = diag_factor[0]
    inverse = diag_inverse[0]
    width = lower.shape[0]
    rows_dev = diag_cotangent.shape[1]
    slot_count = factors.shape[0]
    column = lax.axis_index("col")
    groups = lax.axis_size("col")
    tile = lax.axis_index(TILE)
    core = lax.axis_index("core")
    row_start = tile * rows_dev
    live_slot = jnp.arange(slot_count) < tile_count[0, 0]
    link_flag = live_slot & (tile_rows[0, 0] == column + 1)
    solved = jnp.einsum("sij,jk->sik", cotangent, inverse, preferred_element_type=jnp.float32)
    rounded = jnp.where(
        live_slot[:, None, None], solved.astype(jnp.bfloat16), jnp.zeros_like(cotangent)
    )
    panel_terms = -jnp.einsum("sij,sik->jk", rounded, factors, preferred_element_type=jnp.float32)
    own_rows = lax.dynamic_slice_in_dim(panel_terms, row_start, rows_dev, 0) + diag_cotangent[0]
    panel_terms = lax.dynamic_update_slice_in_dim(panel_terms, own_rows, row_start, 0)
    chosen = jnp.sum(jnp.where(link_flag[:, None, None], factors, jnp.zeros_like(factors)), axis=0)
    link_part = jnp.dot(chosen, inverse, preferred_element_type=jnp.float32)
    reduced = all_sum(jnp.concatenate([panel_terms, link_part], axis=0))
    summed = reduced[:width]
    link_wide = reduced[width:]
    inverse_wide = inverse.astype(jnp.float32)
    curvature = jnp.dot(lower.astype(jnp.float32).T, summed, precision=full)
    symmetric = symmetrize(curvature)
    own_map = 0.5 * jnp.dot(
        inverse_wide.T, jnp.dot(symmetric, inverse_wide, precision=full), precision=full
    )
    half = width // 2
    down = [(i, i - 1) for i in range(1, groups)]

    def sweep(_, incoming):
        advanced = own_map + jnp.dot(
            link_wide.T, jnp.dot(incoming, link_wide, precision=chain), precision=chain
        )
        mine = lax.dynamic_slice_in_dim(advanced, core * half, half, 0)
        arrived = lax.ppermute(mine, "col", down)
        other = swap_cores(arrived)
        whole = jnp.zeros((width, width), jnp.float32)
        whole = lax.dynamic_update_slice_in_dim(whole, arrived, core * half, 0)
        return lax.dynamic_update_slice_in_dim(whole, other, (1 - core) * half, 0)

    incoming = lax.fori_loop(0, groups - 1, sweep, jnp.zeros((width, width), jnp.float32))
    product = jnp.dot(incoming, link_wide, precision=chain)
    link_rows = lax.dynamic_slice_in_dim(link_wide, row_start, rows_dev, 1)
    own_part = lax.dynamic_slice_in_dim(own_map, row_start, rows_dev, 0)
    diag_rows = own_part + jnp.dot(link_rows.T, product, precision=chain)
    adjusted = (solved - 2.0 * product[None]).astype(jnp.bfloat16)
    panel_out = jnp.where(link_flag[:, None, None], adjusted, rounded)
    return (panel_out[None, None], diag_rows[None])


def solution(mesh):
    cols, tiles = mesh.devices.shape
    split = Mesh(mesh.devices.reshape(cols, tiles // 8, 4, 2), ("col",) + TILE)
    in_specs = (
        P("col", TILE, None, None, None),
        P("col", TILE, None, None, None),
        P("col", None, None),
        P("col", None, None),
        P("col", TILE, None),
        P("col", TILE),
        P("col", TILE, None),
    )
    out_specs = (P("col", TILE, None, None, None), P("col", TILE, None))
    return jax.shard_map(
        on_device, mesh=split, in_specs=in_specs, out_specs=out_specs, check_vma=False
    )
```

```python
import jax
import jax.numpy as jnp
from jax import lax
from jax.sharding import Mesh
from jax.sharding import PartitionSpec as P

TILE = ("y", "x", "core")
CHIPS = ("y", "x")


def swap_cores(value):
    return lax.ppermute(value, "core", [(0, 1), (1, 0)])


def all_sum(value):
    core = lax.axis_index("core")
    half = value.shape[0] // 2
    keep = lax.dynamic_slice_in_dim(value, core * half, half, 0)
    send = lax.dynamic_slice_in_dim(value, (1 - core) * half, half, 0)
    mine = keep + swap_cores(send)
    count = lax.axis_size(CHIPS)
    pieces = mine.reshape((count, half // count) + mine.shape[1:])
    share = jnp.sum(lax.all_to_all(pieces, CHIPS, 0, 0), axis=0)
    spread = jnp.broadcast_to(share[None], pieces.shape)
    mine = lax.all_to_all(spread, CHIPS, 0, 0).reshape(mine.shape)
    other = swap_cores(mine)
    whole = jnp.zeros(value.shape, value.dtype)
    whole = lax.dynamic_update_slice_in_dim(whole, mine, core * half, 0)
    return lax.dynamic_update_slice_in_dim(whole, other, (1 - core) * half, 0)


BLOCKS = 4


def pack(matrix):
    size = matrix.shape[0] // BLOCKS
    return jnp.concatenate(
        [
            matrix[i * size : (i + 1) * size, j * size : (j + 1) * size]
            for i in range(BLOCKS)
            for j in range(i + 1)
        ],
        axis=0,
    )


def unpack(packed, width):
    size = width // BLOCKS
    blocks = {}
    k = 0
    for i in range(BLOCKS):
        for j in range(i + 1):
            blocks[i, j] = packed[k * size : (k + 1) * size]
            k += 1
    rows = [
        jnp.concatenate(
            [blocks[i, j] if i >= j else blocks[j, i].T for j in range(BLOCKS)], axis=1
        )
        for i in range(BLOCKS)
    ]
    return jnp.concatenate(rows, axis=0)


def symmetrize(matrix):
    rows = lax.broadcasted_iota(jnp.int32, matrix.shape, 0)
    cols = lax.broadcasted_iota(jnp.int32, matrix.shape, 1)
    return jnp.where(rows >= cols, matrix, matrix.T)


def on_device(
    panel_factor, panel_cotangent, diag_factor, diag_inverse, diag_cotangent, tile_count, tile_rows
):
    full = lax.Precision.HIGHEST
    chain = lax.Precision.HIGH
    factors = panel_factor[0, 0]
    cotangent = panel_cotangent[0, 0]
    lower = diag_factor[0]
    inverse = diag_inverse[0]
    width = lower.shape[0]
    rows_dev = diag_cotangent.shape[1]
    slot_count = factors.shape[0]
    column = lax.axis_index("col")
    groups = lax.axis_size("col")
    tile = lax.axis_index(TILE)
    core = lax.axis_index("core")
    row_start = tile * rows_dev
    live_slot = jnp.arange(slot_count) < tile_count[0, 0]
    link_flag = live_slot & (tile_rows[0, 0] == column + 1)
    solved = jnp.einsum("sij,jk->sik", cotangent, inverse, preferred_element_type=jnp.float32)
    rounded = jnp.where(
        live_slot[:, None, None], solved.astype(jnp.bfloat16), jnp.zeros_like(cotangent)
    )
    panel_terms = -jnp.einsum("sij,sik->jk", rounded, factors, preferred_element_type=jnp.float32)
    own_rows = lax.dynamic_slice_in_dim(panel_terms, row_start, rows_dev, 0) + diag_cotangent[0]
    panel_terms = lax.dynamic_update_slice_in_dim(panel_terms, own_rows, row_start, 0)
    chosen = jnp.sum(jnp.where(link_flag[:, None, None], factors, jnp.zeros_like(factors)), axis=0)
    link_part = jnp.dot(chosen, inverse, preferred_element_type=jnp.float32)
    reduced = all_sum(jnp.concatenate([panel_terms, link_part], axis=0))
    summed = reduced[:width]
    link_wide = reduced[width:]
    inverse_wide = inverse.astype(jnp.float32)
    curvature = jnp.dot(lower.astype(jnp.float32).T, summed, precision=full)
    symmetric = symmetrize(curvature)
    own_map = 0.5 * jnp.dot(
        inverse_wide.T, jnp.dot(symmetric, inverse_wide, precision=full), precision=full
    )
    down = [(2 * i, 2 * (i - 1)) for i in range(1, groups)]

    def sweep(_, packed):
        incoming = unpack(packed, width)
        advanced = own_map + jnp.dot(
            link_wide.T, jnp.dot(incoming, link_wide, precision=chain), precision=chain
        )
        return lax.ppermute(pack(advanced), ("col", "core"), down)

    start = jnp.zeros((BLOCKS * (BLOCKS + 1) // 2 * width // BLOCKS, width // BLOCKS), jnp.float32)
    packed = lax.fori_loop(0, groups - 1, sweep, start)
    shared = lax.ppermute(packed, "core", [(0, 1)])
    incoming = unpack(jnp.where(core == 0, packed, shared), width)
    product = jnp.dot(incoming, link_wide, precision=chain)
    link_rows = lax.dynamic_slice_in_dim(link_wide, row_start, rows_dev, 1)
    own_part = lax.dynamic_slice_in_dim(own_map, row_start, rows_dev, 0)
    diag_rows = own_part + jnp.dot(link_rows.T, product, precision=chain)
    adjusted = (solved - 2.0 * product[None]).astype(jnp.bfloat16)
    panel_out = jnp.where(link_flag[:, None, None], adjusted, rounded)
    return (panel_out[None, None], diag_rows[None])


def solution(mesh):
    cols, tiles = mesh.devices.shape
    split = Mesh(mesh.devices.reshape(cols, tiles // 8, 4, 2), ("col",) + TILE)
    in_specs = (
        P("col", TILE, None, None, None),
        P("col", TILE, None, None, None),
        P("col", None, None),
        P("col", None, None),
        P("col", TILE, None),
        P("col", TILE),
        P("col", TILE, None),
    )
    out_specs = (P("col", TILE, None, None, None), P("col", TILE, None))
    return jax.shard_map(
        on_device, mesh=split, in_specs=in_specs, out_specs=out_specs, check_vma=False
    )
```

```python
import jax
import jax.numpy as jnp
from jax import lax
from jax.sharding import Mesh
from jax.sharding import PartitionSpec as P

TILE = ("y", "x", "core")
CHIPS = ("y", "x")


def swap_cores(value):
    return lax.ppermute(value, "core", [(0, 1), (1, 0)])


def scatter_sum(value, axis):
    count = lax.axis_size(axis)
    pieces = value.reshape((count, value.shape[0] // count) + value.shape[1:])
    return jnp.sum(lax.all_to_all(pieces, axis, 0, 0), axis=0)


def gather_all(value, axis):
    count = lax.axis_size(axis)
    spread = jnp.broadcast_to(value[None], (count,) + value.shape)
    gathered = lax.all_to_all(spread, axis, 0, 0)
    return gathered.reshape((count * value.shape[0],) + value.shape[1:])


def all_sum(value):
    core = lax.axis_index("core")
    half = value.shape[0] // 2
    keep = lax.dynamic_slice_in_dim(value, core * half, half, 0)
    send = lax.dynamic_slice_in_dim(value, (1 - core) * half, half, 0)
    mine = keep + swap_cores(send)
    for axis in CHIPS[::-1]:
        mine = scatter_sum(mine, axis)
    for axis in CHIPS:
        mine = gather_all(mine, axis)
    other = swap_cores(mine)
    whole = jnp.zeros(value.shape, value.dtype)
    whole = lax.dynamic_update_slice_in_dim(whole, mine, core * half, 0)
    return lax.dynamic_update_slice_in_dim(whole, other, (1 - core) * half, 0)


BLOCKS = 4


def pack(matrix):
    size = matrix.shape[0] // BLOCKS
    return jnp.concatenate(
        [
            matrix[i * size : (i + 1) * size, j * size : (j + 1) * size]
            for i in range(BLOCKS)
            for j in range(i + 1)
        ],
        axis=0,
    )


def unpack(packed, width):
    size = width // BLOCKS
    blocks = {}
    k = 0
    for i in range(BLOCKS):
        for j in range(i + 1):
            blocks[i, j] = packed[k * size : (k + 1) * size]
            k += 1
    rows = [
        jnp.concatenate(
            [blocks[i, j] if i >= j else blocks[j, i].T for j in range(BLOCKS)], axis=1
        )
        for i in range(BLOCKS)
    ]
    return jnp.concatenate(rows, axis=0)


def symmetrize(matrix):
    rows = lax.broadcasted_iota(jnp.int32, matrix.shape, 0)
    cols = lax.broadcasted_iota(jnp.int32, matrix.shape, 1)
    return jnp.where(rows >= cols, matrix, matrix.T)


def on_device(
    panel_factor, panel_cotangent, diag_factor, diag_inverse, diag_cotangent, tile_count, tile_rows
):
    full = lax.Precision.HIGHEST
    chain = lax.Precision.HIGH
    factors = panel_factor[0, 0]
    cotangent = panel_cotangent[0, 0]
    lower = diag_factor[0]
    inverse = diag_inverse[0]
    width = lower.shape[0]
    rows_dev = diag_cotangent.shape[1]
    slot_count = factors.shape[0]
    column = lax.axis_index("col")
    groups = lax.axis_size("col")
    tile = lax.axis_index(TILE)
    core = lax.axis_index("core")
    row_start = tile * rows_dev
    live_slot = jnp.arange(slot_count) < tile_count[0, 0]
    link_flag = live_slot & (tile_rows[0, 0] == column + 1)
    solved = jnp.einsum("sij,jk->sik", cotangent, inverse, preferred_element_type=jnp.float32)
    rounded = jnp.where(
        live_slot[:, None, None], solved.astype(jnp.bfloat16), jnp.zeros_like(cotangent)
    )
    panel_terms = -jnp.einsum("sij,sik->jk", rounded, factors, preferred_element_type=jnp.float32)
    own_rows = lax.dynamic_slice_in_dim(panel_terms, row_start, rows_dev, 0) + diag_cotangent[0]
    panel_terms = lax.dynamic_update_slice_in_dim(panel_terms, own_rows, row_start, 0)
    chosen = jnp.sum(jnp.where(link_flag[:, None, None], factors, jnp.zeros_like(factors)), axis=0)
    link_part = jnp.dot(chosen, inverse, preferred_element_type=jnp.float32)
    reduced = all_sum(jnp.concatenate([panel_terms, link_part], axis=0))
    summed = reduced[:width]
    link_wide = reduced[width:]
    inverse_wide = inverse.astype(jnp.float32)
    curvature = jnp.dot(lower.astype(jnp.float32).T, summed, precision=full)
    symmetric = symmetrize(curvature)
    own_map = 0.5 * jnp.dot(
        inverse_wide.T, jnp.dot(symmetric, inverse_wide, precision=full), precision=full
    )
    down = [(2 * i, 2 * (i - 1)) for i in range(1, groups)]

    def sweep(_, packed):
        incoming = unpack(packed, width)
        advanced = own_map + jnp.dot(
            link_wide.T, jnp.dot(incoming, link_wide, precision=chain), precision=chain
        )
        return lax.ppermute(pack(advanced), ("col", "core"), down)

    start = jnp.zeros((BLOCKS * (BLOCKS + 1) // 2 * width // BLOCKS, width // BLOCKS), jnp.float32)
    packed = lax.fori_loop(0, groups - 1, sweep, start)
    shared = lax.ppermute(packed, "core", [(0, 1)])
    incoming = unpack(jnp.where(core == 0, packed, shared), width)
    product = jnp.dot(incoming, link_wide, precision=chain)
    link_rows = lax.dynamic_slice_in_dim(link_wide, row_start, rows_dev, 1)
    own_part = lax.dynamic_slice_in_dim(own_map, row_start, rows_dev, 0)
    diag_rows = own_part + jnp.dot(link_rows.T, product, precision=chain)
    adjusted = (solved - 2.0 * product[None]).astype(jnp.bfloat16)
    panel_out = jnp.where(link_flag[:, None, None], adjusted, rounded)
    return (panel_out[None, None], diag_rows[None])


def solution(mesh):
    cols, tiles = mesh.devices.shape
    split = Mesh(mesh.devices.reshape(cols, tiles // 8, 4, 2), ("col",) + TILE)
    in_specs = (
        P("col", TILE, None, None, None),
        P("col", TILE, None, None, None),
        P("col", None, None),
        P("col", None, None),
        P("col", TILE, None),
        P("col", TILE),
        P("col", TILE, None),
    )
    out_specs = (P("col", TILE, None, None, None), P("col", TILE, None))
    return jax.shard_map(
        on_device, mesh=split, in_specs=in_specs, out_specs=out_specs, check_vma=False
    )
```

```python
import jax
import jax.numpy as jnp
from jax import lax
from jax.sharding import Mesh
from jax.sharding import PartitionSpec as P

TILE = ("y", "x", "core")
CHIPS = ("y", "x")


def swap_cores(value):
    return lax.ppermute(value, "core", [(0, 1), (1, 0)])


def scatter_sum(value, axis):
    count = lax.axis_size(axis)
    pieces = value.reshape((count, value.shape[0] // count) + value.shape[1:])
    return jnp.sum(lax.all_to_all(pieces, axis, 0, 0), axis=0)


def gather_all(value, axis):
    count = lax.axis_size(axis)
    spread = jnp.broadcast_to(value[None], (count,) + value.shape)
    gathered = lax.all_to_all(spread, axis, 0, 0)
    return gathered.reshape((count * value.shape[0],) + value.shape[1:])


def all_sum(value):
    core = lax.axis_index("core")
    half = value.shape[0] // 2
    keep = lax.dynamic_slice_in_dim(value, core * half, half, 0)
    send = lax.dynamic_slice_in_dim(value, (1 - core) * half, half, 0)
    mine = keep + swap_cores(send)
    for axis in CHIPS[::-1]:
        mine = scatter_sum(mine, axis)
    for axis in CHIPS:
        mine = gather_all(mine, axis)
    other = swap_cores(mine)
    whole = jnp.zeros(value.shape, value.dtype)
    whole = lax.dynamic_update_slice_in_dim(whole, mine, core * half, 0)
    return lax.dynamic_update_slice_in_dim(whole, other, (1 - core) * half, 0)


BLOCKS = 4


def pack(matrix):
    size = matrix.shape[0] // BLOCKS
    return jnp.concatenate(
        [
            matrix[i * size : (i + 1) * size, j * size : (j + 1) * size]
            for i in range(BLOCKS)
            for j in range(i + 1)
        ],
        axis=0,
    )


def unpack(packed, width):
    size = width // BLOCKS
    blocks = {}
    k = 0
    for i in range(BLOCKS):
        for j in range(i + 1):
            blocks[i, j] = packed[k * size : (k + 1) * size]
            k += 1
    rows = [
        jnp.concatenate(
            [blocks[i, j] if i >= j else blocks[j, i].T for j in range(BLOCKS)], axis=1
        )
        for i in range(BLOCKS)
    ]
    return jnp.concatenate(rows, axis=0)


def symmetrize(matrix):
    rows = lax.broadcasted_iota(jnp.int32, matrix.shape, 0)
    cols = lax.broadcasted_iota(jnp.int32, matrix.shape, 1)
    return jnp.where(rows >= cols, matrix, matrix.T)


def on_device(
    panel_factor, panel_cotangent, diag_factor, diag_inverse, diag_cotangent, tile_count, tile_rows
):
    chain = lax.Precision.HIGH
    factors = panel_factor[0, 0]
    cotangent = panel_cotangent[0, 0]
    lower = diag_factor[0]
    inverse = diag_inverse[0]
    width = lower.shape[0]
    rows_dev = diag_cotangent.shape[1]
    slot_count = factors.shape[0]
    column = lax.axis_index("col")
    groups = lax.axis_size("col")
    tile = lax.axis_index(TILE)
    core = lax.axis_index("core")
    row_start = tile * rows_dev
    live_slot = jnp.arange(slot_count) < tile_count[0, 0]
    link_flag = live_slot & (tile_rows[0, 0] == column + 1)
    solved = jnp.einsum("sij,jk->sik", cotangent, inverse, preferred_element_type=jnp.float32)
    rounded = jnp.where(
        live_slot[:, None, None], solved.astype(jnp.bfloat16), jnp.zeros_like(cotangent)
    )
    panel_terms = -jnp.einsum("sij,sik->jk", rounded, factors, preferred_element_type=jnp.float32)
    own_rows = lax.dynamic_slice_in_dim(panel_terms, row_start, rows_dev, 0) + diag_cotangent[0]
    panel_terms = lax.dynamic_update_slice_in_dim(panel_terms, own_rows, row_start, 0)
    chosen = jnp.sum(jnp.where(link_flag[:, None, None], factors, jnp.zeros_like(factors)), axis=0)
    link_part = jnp.dot(chosen, inverse, preferred_element_type=jnp.float32)
    reduced = all_sum(jnp.concatenate([panel_terms, link_part], axis=0))
    summed = reduced[:width]
    link_wide = reduced[width:]
    inverse_wide = inverse.astype(jnp.float32)
    curvature = jnp.dot(lower.astype(jnp.float32).T, summed, precision=chain)
    symmetric = symmetrize(curvature)
    own_map = 0.5 * jnp.dot(
        inverse_wide.T, jnp.dot(symmetric, inverse_wide, precision=chain), precision=chain
    )
    down = [(2 * i, 2 * (i - 1)) for i in range(1, groups)]

    packed = lax.ppermute(pack(own_map), ("col", "core"), down)
    for _ in range(groups - 2):
        incoming = unpack(packed, width)
        advanced = own_map + jnp.dot(
            link_wide.T, jnp.dot(incoming, link_wide, precision=chain), precision=chain
        )
        packed = lax.ppermute(pack(advanced), ("col", "core"), down)
    shared = lax.ppermute(packed, "core", [(0, 1)])
    incoming = unpack(jnp.where(core == 0, packed, shared), width)
    product = jnp.dot(incoming, link_wide, precision=chain)
    link_rows = lax.dynamic_slice_in_dim(link_wide, row_start, rows_dev, 1)
    own_part = lax.dynamic_slice_in_dim(own_map, row_start, rows_dev, 0)
    diag_rows = own_part + jnp.dot(link_rows.T, product, precision=chain)
    adjusted = (solved - 2.0 * product[None]).astype(jnp.bfloat16)
    panel_out = jnp.where(link_flag[:, None, None], adjusted, rounded)
    return (panel_out[None, None], diag_rows[None])


def solution(mesh):
    cols, tiles = mesh.devices.shape
    split = Mesh(mesh.devices.reshape(cols, tiles // 8, 4, 2), ("col",) + TILE)
    in_specs = (
        P("col", TILE, None, None, None),
        P("col", TILE, None, None, None),
        P("col", None, None),
        P("col", None, None),
        P("col", TILE, None),
        P("col", TILE),
        P("col", TILE, None),
    )
    out_specs = (P("col", TILE, None, None, None), P("col", TILE, None))
    return jax.shard_map(
        on_device, mesh=split, in_specs=in_specs, out_specs=out_specs, check_vma=False
    )
```

```python
import jax
import jax.numpy as jnp
from jax import lax
from jax.sharding import Mesh
from jax.sharding import PartitionSpec as P

TILE = ("y", "x", "core")
CHIPS = ("y", "x")


def swap_cores(value):
    return lax.ppermute(value, "core", [(0, 1), (1, 0)])


def scatter_sum(value, axis):
    count = lax.axis_size(axis)
    pieces = value.reshape((count, value.shape[0] // count) + value.shape[1:])
    return jnp.sum(lax.all_to_all(pieces, axis, 0, 0), axis=0)


def gather_all(value, axis):
    count = lax.axis_size(axis)
    spread = jnp.broadcast_to(value[None], (count,) + value.shape)
    gathered = lax.all_to_all(spread, axis, 0, 0)
    return gathered.reshape((count * value.shape[0],) + value.shape[1:])


def all_sum(value):
    core = lax.axis_index("core")
    half = value.shape[0] // 2
    keep = lax.dynamic_slice_in_dim(value, core * half, half, 0)
    send = lax.dynamic_slice_in_dim(value, (1 - core) * half, half, 0)
    mine = keep + swap_cores(send)
    for axis in CHIPS[::-1]:
        mine = scatter_sum(mine, axis)
    for axis in CHIPS:
        mine = gather_all(mine, axis)
    return mine


BLOCKS = 4


def pack(matrix):
    size = matrix.shape[0] // BLOCKS
    return jnp.concatenate(
        [
            matrix[i * size : (i + 1) * size, j * size : (j + 1) * size]
            for i in range(BLOCKS)
            for j in range(i + 1)
        ],
        axis=0,
    )


def unpack(packed, width):
    size = width // BLOCKS
    blocks = {}
    k = 0
    for i in range(BLOCKS):
        for j in range(i + 1):
            blocks[i, j] = packed[k * size : (k + 1) * size]
            k += 1
    rows = [
        jnp.concatenate(
            [blocks[i, j] if i >= j else blocks[j, i].T for j in range(BLOCKS)], axis=1
        )
        for i in range(BLOCKS)
    ]
    return jnp.concatenate(rows, axis=0)


def symmetrize(matrix):
    rows = lax.broadcasted_iota(jnp.int32, matrix.shape, 0)
    cols = lax.broadcasted_iota(jnp.int32, matrix.shape, 1)
    return jnp.where(rows >= cols, matrix, matrix.T)


def on_device(
    panel_factor, panel_cotangent, diag_factor, diag_inverse, diag_cotangent, tile_count, tile_rows
):
    chain = lax.Precision.HIGH
    factors = panel_factor[0, 0]
    cotangent = panel_cotangent[0, 0]
    lower = diag_factor[0]
    inverse = diag_inverse[0]
    width = lower.shape[0]
    rows_dev = diag_cotangent.shape[1]
    slot_count = factors.shape[0]
    column = lax.axis_index("col")
    groups = lax.axis_size("col")
    tile = lax.axis_index(TILE)
    core = lax.axis_index("core")
    row_start = tile * rows_dev
    live_slot = jnp.arange(slot_count) < tile_count[0, 0]
    link_flag = live_slot & (tile_rows[0, 0] == column + 1)
    solved = jnp.einsum("sij,jk->sik", cotangent, inverse, preferred_element_type=jnp.float32)
    rounded = jnp.where(
        live_slot[:, None, None], solved.astype(jnp.bfloat16), jnp.zeros_like(cotangent)
    )
    panel_terms = -jnp.einsum("sij,sik->jk", rounded, factors, preferred_element_type=jnp.float32)
    own_rows = lax.dynamic_slice_in_dim(panel_terms, row_start, rows_dev, 0) + diag_cotangent[0]
    panel_terms = lax.dynamic_update_slice_in_dim(panel_terms, own_rows, row_start, 0)
    chosen = jnp.sum(jnp.where(link_flag[:, None, None], factors, jnp.zeros_like(factors)), axis=0)
    link_part = jnp.dot(chosen, inverse, preferred_element_type=jnp.float32)
    mine = all_sum(jnp.concatenate([panel_terms, link_part], axis=0))
    other = swap_cores(mine)
    link_wide = jnp.where(core == 0, other, mine)
    inverse_wide = inverse.astype(jnp.float32)
    lower_wide = lower.astype(jnp.float32)

    def own_of(summed):
        symmetric = symmetrize(jnp.dot(lower_wide.T, summed, precision=chain))
        return 0.5 * jnp.dot(
            inverse_wide.T, jnp.dot(symmetric, inverse_wide, precision=chain), precision=chain
        )

    chain_own = own_of(mine)
    down = [(2 * i, 2 * (i - 1)) for i in range(1, groups)]

    def sweep(_, packed):
        incoming = unpack(packed, width)
        advanced = chain_own + jnp.dot(
            link_wide.T, jnp.dot(incoming, link_wide, precision=chain), precision=chain
        )
        return lax.ppermute(pack(advanced), ("col", "core"), down)

    first = lax.ppermute(pack(chain_own), ("col", "core"), down)
    packed = lax.fori_loop(0, groups - 2, sweep, first)
    own_map = jnp.where(core == 0, chain_own, own_of(other))
    shared = lax.ppermute(packed, "core", [(0, 1)])
    incoming = unpack(jnp.where(core == 0, packed, shared), width)
    product = jnp.dot(incoming, link_wide, precision=chain)
    link_rows = lax.dynamic_slice_in_dim(link_wide, row_start, rows_dev, 1)
    own_part = lax.dynamic_slice_in_dim(own_map, row_start, rows_dev, 0)
    diag_rows = own_part + jnp.dot(link_rows.T, product, precision=chain)
    adjusted = (solved - 2.0 * product[None]).astype(jnp.bfloat16)
    panel_out = jnp.where(link_flag[:, None, None], adjusted, rounded)
    return (panel_out[None, None], diag_rows[None])


def solution(mesh):
    cols, tiles = mesh.devices.shape
    split = Mesh(mesh.devices.reshape(cols, tiles // 8, 4, 2), ("col",) + TILE)
    in_specs = (
        P("col", TILE, None, None, None),
        P("col", TILE, None, None, None),
        P("col", None, None),
        P("col", None, None),
        P("col", TILE, None),
        P("col", TILE),
        P("col", TILE, None),
    )
    out_specs = (P("col", TILE, None, None, None), P("col", TILE, None))
    return jax.shard_map(
        on_device, mesh=split, in_specs=in_specs, out_specs=out_specs, check_vma=False
    )
```

```python
import jax
import jax.numpy as jnp
from jax import lax
from jax.sharding import Mesh
from jax.sharding import PartitionSpec as P

TILE = ("y", "x", "core")
CHIPS = ("y", "x")


def swap_cores(value):
    return lax.ppermute(value, "core", [(0, 1), (1, 0)])


def scatter_sum(value, axis):
    count = lax.axis_size(axis)
    pieces = value.reshape((count, value.shape[0] // count) + value.shape[1:])
    return jnp.sum(lax.all_to_all(pieces, axis, 0, 0), axis=0)


def gather_all(value, axis):
    count = lax.axis_size(axis)
    spread = jnp.broadcast_to(value[None], (count,) + value.shape)
    gathered = lax.all_to_all(spread, axis, 0, 0)
    return gathered.reshape((count * value.shape[0],) + value.shape[1:])


def all_sum(value):
    core = lax.axis_index("core")
    half = value.shape[0] // 2
    keep = lax.dynamic_slice_in_dim(value, core * half, half, 0)
    send = lax.dynamic_slice_in_dim(value, (1 - core) * half, half, 0)
    mine = keep + swap_cores(send)
    for axis in CHIPS[::-1]:
        mine = scatter_sum(mine, axis)
    for axis in CHIPS:
        mine = gather_all(mine, axis)
    return mine


BLOCKS = 4


def pack(matrix):
    size = matrix.shape[0] // BLOCKS
    return jnp.concatenate(
        [
            matrix[i * size : (i + 1) * size, j * size : (j + 1) * size]
            for i in range(BLOCKS)
            for j in range(i + 1)
        ],
        axis=0,
    )


def unpack(packed, width):
    size = width // BLOCKS
    zero = jnp.zeros((size, size), packed.dtype)
    blocks = {}
    k = 0
    for i in range(BLOCKS):
        for j in range(i + 1):
            blocks[i, j] = packed[k * size : (k + 1) * size]
            k += 1
    lower = jnp.concatenate(
        [
            jnp.concatenate([blocks[i, j] if i >= j else zero for j in range(BLOCKS)], axis=1)
            for i in range(BLOCKS)
        ],
        axis=0,
    )
    rows = lax.broadcasted_iota(jnp.int32, lower.shape, 0) // size
    cols = lax.broadcasted_iota(jnp.int32, lower.shape, 1) // size
    return jnp.where(rows >= cols, lower, lower.T)


def symmetrize(matrix):
    rows = lax.broadcasted_iota(jnp.int32, matrix.shape, 0)
    cols = lax.broadcasted_iota(jnp.int32, matrix.shape, 1)
    return jnp.where(rows >= cols, matrix, matrix.T)


def on_device(
    panel_factor, panel_cotangent, diag_factor, diag_inverse, diag_cotangent, tile_count, tile_rows
):
    chain = lax.Precision.HIGH
    factors = panel_factor[0, 0]
    cotangent = panel_cotangent[0, 0]
    lower = diag_factor[0]
    inverse = diag_inverse[0]
    width = lower.shape[0]
    rows_dev = diag_cotangent.shape[1]
    slot_count = factors.shape[0]
    column = lax.axis_index("col")
    groups = lax.axis_size("col")
    tile = lax.axis_index(TILE)
    core = lax.axis_index("core")
    row_start = tile * rows_dev
    live_slot = jnp.arange(slot_count) < tile_count[0, 0]
    link_flag = live_slot & (tile_rows[0, 0] == column + 1)
    solved = jnp.einsum("sij,jk->sik", cotangent, inverse, preferred_element_type=jnp.float32)
    rounded = jnp.where(
        live_slot[:, None, None], solved.astype(jnp.bfloat16), jnp.zeros_like(cotangent)
    )
    panel_terms = -jnp.einsum("sij,sik->jk", rounded, factors, preferred_element_type=jnp.float32)
    own_rows = lax.dynamic_slice_in_dim(panel_terms, row_start, rows_dev, 0) + diag_cotangent[0]
    panel_terms = lax.dynamic_update_slice_in_dim(panel_terms, own_rows, row_start, 0)
    chosen = jnp.sum(jnp.where(link_flag[:, None, None], factors, jnp.zeros_like(factors)), axis=0)
    link_part = jnp.dot(chosen, inverse, preferred_element_type=jnp.float32)
    mine = all_sum(jnp.concatenate([panel_terms, link_part], axis=0))
    other = swap_cores(mine)
    link_wide = jnp.where(core == 0, other, mine)
    inverse_wide = inverse.astype(jnp.float32)
    lower_wide = lower.astype(jnp.float32)

    def own_of(summed):
        symmetric = symmetrize(jnp.dot(lower_wide.T, summed, precision=chain))
        return 0.5 * jnp.dot(
            inverse_wide.T, jnp.dot(symmetric, inverse_wide, precision=chain), precision=chain
        )

    chain_own = own_of(mine)
    down = [(2 * i, 2 * (i - 1)) for i in range(1, groups)]

    def sweep(_, packed):
        incoming = unpack(packed, width)
        advanced = chain_own + jnp.dot(
            link_wide.T, jnp.dot(incoming, link_wide, precision=chain), precision=chain
        )
        return lax.ppermute(pack(advanced), ("col", "core"), down)

    start = jnp.zeros((BLOCKS * (BLOCKS + 1) // 2 * width // BLOCKS, width // BLOCKS), jnp.float32)
    packed = lax.fori_loop(0, groups - 1, sweep, start)
    own_map = jnp.where(core == 0, chain_own, own_of(other))
    shared = lax.ppermute(packed, "core", [(0, 1)])
    incoming = unpack(jnp.where(core == 0, packed, shared), width)
    product = jnp.dot(incoming, link_wide, precision=chain)
    link_rows = lax.dynamic_slice_in_dim(link_wide, row_start, rows_dev, 1)
    own_part = lax.dynamic_slice_in_dim(own_map, row_start, rows_dev, 0)
    diag_rows = own_part + jnp.dot(link_rows.T, product, precision=chain)
    adjusted = (solved - 2.0 * product[None]).astype(jnp.bfloat16)
    panel_out = jnp.where(link_flag[:, None, None], adjusted, rounded)
    return (panel_out[None, None], diag_rows[None])


def solution(mesh):
    cols, tiles = mesh.devices.shape
    split = Mesh(mesh.devices.reshape(cols, tiles // 8, 4, 2), ("col",) + TILE)
    in_specs = (
        P("col", TILE, None, None, None),
        P("col", TILE, None, None, None),
        P("col", None, None),
        P("col", None, None),
        P("col", TILE, None),
        P("col", TILE),
        P("col", TILE, None),
    )
    out_specs = (P("col", TILE, None, None, None), P("col", TILE, None))
    return jax.shard_map(
        on_device, mesh=split, in_specs=in_specs, out_specs=out_specs, check_vma=False
    )
```

```python
import jax
import jax.numpy as jnp
from jax import lax
from jax.sharding import Mesh
from jax.sharding import PartitionSpec as P

TILE = ("y", "x", "core")
CHIPS = ("y", "x")


def swap_cores(value):
    return lax.ppermute(value, "core", [(0, 1), (1, 0)])


def scatter_sum(value, axis):
    count = lax.axis_size(axis)
    pieces = value.reshape((count, value.shape[0] // count) + value.shape[1:])
    return jnp.sum(lax.all_to_all(pieces, axis, 0, 0), axis=0)


def gather_all(value, axis):
    count = lax.axis_size(axis)
    spread = jnp.broadcast_to(value[None], (count,) + value.shape)
    gathered = lax.all_to_all(spread, axis, 0, 0)
    return gathered.reshape((count * value.shape[0],) + value.shape[1:])


def all_sum(value):
    core = lax.axis_index("core")
    half = value.shape[0] // 2
    keep = lax.dynamic_slice_in_dim(value, core * half, half, 0)
    send = lax.dynamic_slice_in_dim(value, (1 - core) * half, half, 0)
    mine = keep + swap_cores(send)
    for axis in CHIPS[::-1]:
        mine = scatter_sum(mine, axis)
    for axis in CHIPS:
        mine = gather_all(mine, axis)
    return mine


BLOCKS = 4


def pack(matrix):
    size = matrix.shape[0] // BLOCKS
    return jnp.concatenate(
        [
            matrix[i * size : (i + 1) * size, j * size : (j + 1) * size]
            for i in range(BLOCKS)
            for j in range(i + 1)
        ],
        axis=0,
    )


def unpack(packed, width):
    size = width // BLOCKS
    blocks = {}
    k = 0
    for i in range(BLOCKS):
        for j in range(i + 1):
            blocks[i, j] = packed[k * size : (k + 1) * size]
            k += 1
    rows = [
        jnp.concatenate(
            [blocks[i, j] if i >= j else blocks[j, i].T for j in range(BLOCKS)], axis=1
        )
        for i in range(BLOCKS)
    ]
    return jnp.concatenate(rows, axis=0)


def symmetrize(matrix):
    rows = lax.broadcasted_iota(jnp.int32, matrix.shape, 0)
    cols = lax.broadcasted_iota(jnp.int32, matrix.shape, 1)
    return jnp.where(rows >= cols, matrix, matrix.T)


def on_device(
    panel_factor, panel_cotangent, diag_factor, diag_inverse, diag_cotangent, tile_count, tile_rows
):
    chain = lax.Precision.HIGH
    factors = panel_factor[0, 0]
    cotangent = panel_cotangent[0, 0]
    lower = diag_factor[0]
    inverse = diag_inverse[0]
    width = lower.shape[0]
    rows_dev = diag_cotangent.shape[1]
    slot_count = factors.shape[0]
    column = lax.axis_index("col")
    groups = lax.axis_size("col")
    tile = lax.axis_index(TILE)
    core = lax.axis_index("core")
    row_start = tile * rows_dev
    live_slot = jnp.arange(slot_count) < tile_count[0, 0]
    link_flag = live_slot & (tile_rows[0, 0] == column + 1)
    solved = jnp.einsum("sij,jk->sik", cotangent, inverse, preferred_element_type=jnp.float32)
    rounded = jnp.where(
        live_slot[:, None, None], solved.astype(jnp.bfloat16), jnp.zeros_like(cotangent)
    )
    panel_terms = -jnp.einsum("sij,sik->jk", rounded, factors, preferred_element_type=jnp.float32)
    own_rows = lax.dynamic_slice_in_dim(panel_terms, row_start, rows_dev, 0) + diag_cotangent[0]
    panel_terms = lax.dynamic_update_slice_in_dim(panel_terms, own_rows, row_start, 0)
    chosen = jnp.sum(jnp.where(link_flag[:, None, None], factors, jnp.zeros_like(factors)), axis=0)
    link_part = jnp.dot(chosen, inverse, preferred_element_type=jnp.float32)
    mine = all_sum(jnp.concatenate([panel_terms, link_part], axis=0))
    other = swap_cores(mine)
    link_wide = jnp.where(core == 0, other, mine)
    inverse_wide = inverse.astype(jnp.float32)
    lower_wide = lower.astype(jnp.float32)

    def own_of(summed):
        symmetric = symmetrize(jnp.dot(lower_wide.T, summed, precision=chain))
        return 0.5 * jnp.dot(
            inverse_wide.T, jnp.dot(symmetric, inverse_wide, precision=chain), precision=chain
        )

    chain_own = own_of(mine)
    down = [(2 * i, 2 * (i - 1)) for i in range(1, groups)]

    def sweep(_, packed):
        incoming = unpack(packed, width)
        advanced = chain_own + jnp.dot(
            link_wide.T, jnp.dot(incoming, link_wide, precision=chain), precision=chain
        )
        return lax.ppermute(pack(advanced), ("col", "core"), down)

    start = jnp.zeros((BLOCKS * (BLOCKS + 1) // 2 * width // BLOCKS, width // BLOCKS), jnp.float32)
    packed = lax.fori_loop(0, groups - 1, sweep, start)
    own_map = jnp.where(core == 0, chain_own, lax.ppermute(chain_own, "core", [(0, 1)]))
    shared = lax.ppermute(packed, "core", [(0, 1)])
    incoming = unpack(jnp.where(core == 0, packed, shared), width)
    product = jnp.dot(incoming, link_wide, precision=chain)
    link_rows = lax.dynamic_slice_in_dim(link_wide, row_start, rows_dev, 1)
    own_part = lax.dynamic_slice_in_dim(own_map, row_start, rows_dev, 0)
    diag_rows = own_part + jnp.dot(link_rows.T, product, precision=chain)
    adjusted = (solved - 2.0 * product[None]).astype(jnp.bfloat16)
    panel_out = jnp.where(link_flag[:, None, None], adjusted, rounded)
    return (panel_out[None, None], diag_rows[None])


def solution(mesh):
    cols, tiles = mesh.devices.shape
    split = Mesh(mesh.devices.reshape(cols, tiles // 8, 4, 2), ("col",) + TILE)
    in_specs = (
        P("col", TILE, None, None, None),
        P("col", TILE, None, None, None),
        P("col", None, None),
        P("col", None, None),
        P("col", TILE, None),
        P("col", TILE),
        P("col", TILE, None),
    )
    out_specs = (P("col", TILE, None, None, None), P("col", TILE, None))
    return jax.shard_map(
        on_device, mesh=split, in_specs=in_specs, out_specs=out_specs, check_vma=False
    )
```

```python
import jax
import jax.numpy as jnp
from jax import lax
from jax.sharding import Mesh
from jax.sharding import PartitionSpec as P

TILE = ("y", "x", "core")
CHIPS = ("y", "x")


def swap_cores(value):
    return lax.ppermute(value, "core", [(0, 1), (1, 0)])


def scatter_sum(value, axis):
    count = lax.axis_size(axis)
    pieces = value.reshape((count, value.shape[0] // count) + value.shape[1:])
    return jnp.sum(lax.all_to_all(pieces, axis, 0, 0), axis=0)


def gather_all(value, axis):
    count = lax.axis_size(axis)
    spread = jnp.broadcast_to(value[None], (count,) + value.shape)
    gathered = lax.all_to_all(spread, axis, 0, 0)
    return gathered.reshape((count * value.shape[0],) + value.shape[1:])


def all_sum(value):
    core = lax.axis_index("core")
    half = value.shape[0] // 2
    keep = lax.dynamic_slice_in_dim(value, core * half, half, 0)
    send = lax.dynamic_slice_in_dim(value, (1 - core) * half, half, 0)
    mine = keep + swap_cores(send)
    for axis in CHIPS:
        mine = scatter_sum(mine, axis)
    for axis in CHIPS[::-1]:
        mine = gather_all(mine, axis)
    return mine


BLOCKS = 4


def pack(matrix):
    size = matrix.shape[0] // BLOCKS
    return jnp.concatenate(
        [
            matrix[i * size : (i + 1) * size, j * size : (j + 1) * size]
            for i in range(BLOCKS)
            for j in range(i + 1)
        ],
        axis=0,
    )


def unpack(packed, width):
    size = width // BLOCKS
    blocks = {}
    k = 0
    for i in range(BLOCKS):
        for j in range(i + 1):
            blocks[i, j] = packed[k * size : (k + 1) * size]
            k += 1
    rows = [
        jnp.concatenate(
            [blocks[i, j] if i >= j else blocks[j, i].T for j in range(BLOCKS)], axis=1
        )
        for i in range(BLOCKS)
    ]
    return jnp.concatenate(rows, axis=0)


def symmetrize(matrix):
    rows = lax.broadcasted_iota(jnp.int32, matrix.shape, 0)
    cols = lax.broadcasted_iota(jnp.int32, matrix.shape, 1)
    return jnp.where(rows >= cols, matrix, matrix.T)


def on_device(
    panel_factor, panel_cotangent, diag_factor, diag_inverse, diag_cotangent, tile_count, tile_rows
):
    chain = lax.Precision.HIGH
    factors = panel_factor[0, 0]
    cotangent = panel_cotangent[0, 0]
    lower = diag_factor[0]
    inverse = diag_inverse[0]
    width = lower.shape[0]
    rows_dev = diag_cotangent.shape[1]
    slot_count = factors.shape[0]
    column = lax.axis_index("col")
    groups = lax.axis_size("col")
    tile = lax.axis_index(TILE)
    core = lax.axis_index("core")
    row_start = tile * rows_dev
    live_slot = jnp.arange(slot_count) < tile_count[0, 0]
    link_flag = live_slot & (tile_rows[0, 0] == column + 1)
    solved = jnp.einsum("sij,jk->sik", cotangent, inverse, preferred_element_type=jnp.float32)
    rounded = jnp.where(
        live_slot[:, None, None], solved.astype(jnp.bfloat16), jnp.zeros_like(cotangent)
    )
    panel_terms = -jnp.einsum("sij,sik->jk", rounded, factors, preferred_element_type=jnp.float32)
    own_rows = lax.dynamic_slice_in_dim(panel_terms, row_start, rows_dev, 0) + diag_cotangent[0]
    panel_terms = lax.dynamic_update_slice_in_dim(panel_terms, own_rows, row_start, 0)
    chosen = jnp.sum(jnp.where(link_flag[:, None, None], factors, jnp.zeros_like(factors)), axis=0)
    link_part = jnp.dot(chosen, inverse, preferred_element_type=jnp.float32)
    mine = all_sum(jnp.concatenate([panel_terms, link_part], axis=0))
    other = swap_cores(mine)
    link_wide = jnp.where(core == 0, other, mine)
    inverse_wide = inverse.astype(jnp.float32)
    lower_wide = lower.astype(jnp.float32)

    def own_of(summed):
        symmetric = symmetrize(jnp.dot(lower_wide.T, summed, precision=chain))
        return 0.5 * jnp.dot(
            inverse_wide.T, jnp.dot(symmetric, inverse_wide, precision=chain), precision=chain
        )

    chain_own = own_of(mine)
    down = [(2 * i, 2 * (i - 1)) for i in range(1, groups)]

    def sweep(_, packed):
        incoming = unpack(packed, width)
        advanced = chain_own + jnp.dot(
            link_wide.T, jnp.dot(incoming, link_wide, precision=chain), precision=chain
        )
        return lax.ppermute(pack(advanced), ("col", "core"), down)

    start = jnp.zeros((BLOCKS * (BLOCKS + 1) // 2 * width // BLOCKS, width // BLOCKS), jnp.float32)
    packed = lax.fori_loop(0, groups - 1, sweep, start)
    own_map = jnp.where(core == 0, chain_own, lax.ppermute(chain_own, "core", [(0, 1)]))
    shared = lax.ppermute(packed, "core", [(0, 1)])
    incoming = unpack(jnp.where(core == 0, packed, shared), width)
    product = jnp.dot(incoming, link_wide, precision=chain)
    link_rows = lax.dynamic_slice_in_dim(link_wide, row_start, rows_dev, 1)
    own_part = lax.dynamic_slice_in_dim(own_map, row_start, rows_dev, 0)
    diag_rows = own_part + jnp.dot(link_rows.T, product, precision=chain)
    adjusted = (solved - 2.0 * product[None]).astype(jnp.bfloat16)
    panel_out = jnp.where(link_flag[:, None, None], adjusted, rounded)
    return (panel_out[None, None], diag_rows[None])


def solution(mesh):
    cols, tiles = mesh.devices.shape
    split = Mesh(mesh.devices.reshape(cols, tiles // 8, 4, 2), ("col",) + TILE)
    in_specs = (
        P("col", TILE, None, None, None),
        P("col", TILE, None, None, None),
        P("col", None, None),
        P("col", None, None),
        P("col", TILE, None),
        P("col", TILE),
        P("col", TILE, None),
    )
    out_specs = (P("col", TILE, None, None, None), P("col", TILE, None))
    return jax.shard_map(
        on_device, mesh=split, in_specs=in_specs, out_specs=out_specs, check_vma=False
    )
```

```python
import jax
import jax.numpy as jnp
from jax import lax
from jax.sharding import Mesh
from jax.sharding import PartitionSpec as P

TILE = ("y", "x", "core")
CHIPS = ("y", "x")


def swap_cores(value):
    return lax.ppermute(value, "core", [(0, 1), (1, 0)])


def scatter_sum(value, axis):
    count = lax.axis_size(axis)
    pieces = value.reshape((count, value.shape[0] // count) + value.shape[1:])
    return jnp.sum(lax.all_to_all(pieces, axis, 0, 0), axis=0)


def gather_all(value, axis):
    count = lax.axis_size(axis)
    spread = jnp.broadcast_to(value[None], (count,) + value.shape)
    gathered = lax.all_to_all(spread, axis, 0, 0)
    return gathered.reshape((count * value.shape[0],) + value.shape[1:])


def all_sum(value):
    core = lax.axis_index("core")
    half = value.shape[0] // 2
    keep = lax.dynamic_slice_in_dim(value, core * half, half, 0)
    send = lax.dynamic_slice_in_dim(value, (1 - core) * half, half, 0)
    mine = keep + swap_cores(send)
    for axis in CHIPS[::-1]:
        mine = scatter_sum(mine, axis)
    for axis in CHIPS:
        mine = gather_all(mine, axis)
    return mine


BLOCKS = 4


def pack(matrix):
    size = matrix.shape[0] // BLOCKS
    block = lambda i, j: matrix[i * size : (i + 1) * size, j * size : (j + 1) * size]
    rows = lax.broadcasted_iota(jnp.int32, (size, size), 0)
    cols = lax.broadcasted_iota(jnp.int32, (size, size), 1)
    parts = [block(i, j) for i in range(BLOCKS) for j in range(i)]
    diagonals = []
    for i in range(0, BLOCKS, 2):
        parts.append(jnp.where(rows >= cols, block(i, i), block(i + 1, i + 1).T))
        diagonals.append(jnp.diagonal(block(i + 1, i + 1)))
    tail = jnp.zeros((8, size), matrix.dtype).at[: len(diagonals)].set(jnp.stack(diagonals))
    return jnp.concatenate(parts + [tail], axis=0)


def unpack(packed, width):
    size = width // BLOCKS
    rows = lax.broadcasted_iota(jnp.int32, (size, size), 0)
    cols = lax.broadcasted_iota(jnp.int32, (size, size), 1)
    blocks = {}
    k = 0
    for i in range(BLOCKS):
        for j in range(i):
            blocks[i, j] = packed[k * size : (k + 1) * size]
            k += 1
    tail = packed[-8:]
    for n, i in enumerate(range(0, BLOCKS, 2)):
        folded = packed[k * size : (k + 1) * size]
        k += 1
        blocks[i, i] = jnp.where(rows >= cols, folded, folded.T)
        blocks[i + 1, i + 1] = jnp.where(
            rows > cols, folded.T, jnp.where(rows < cols, folded, tail[n][None, :])
        )
    rows_of = [
        jnp.concatenate(
            [blocks[i, j] if i >= j else blocks[j, i].T for j in range(BLOCKS)], axis=1
        )
        for i in range(BLOCKS)
    ]
    return jnp.concatenate(rows_of, axis=0)


def symmetrize(matrix):
    rows = lax.broadcasted_iota(jnp.int32, matrix.shape, 0)
    cols = lax.broadcasted_iota(jnp.int32, matrix.shape, 1)
    return jnp.where(rows >= cols, matrix, matrix.T)


def on_device(
    panel_factor, panel_cotangent, diag_factor, diag_inverse, diag_cotangent, tile_count, tile_rows
):
    chain = lax.Precision.HIGH
    factors = panel_factor[0, 0]
    cotangent = panel_cotangent[0, 0]
    lower = diag_factor[0]
    inverse = diag_inverse[0]
    width = lower.shape[0]
    rows_dev = diag_cotangent.shape[1]
    slot_count = factors.shape[0]
    column = lax.axis_index("col")
    groups = lax.axis_size("col")
    tile = lax.axis_index(TILE)
    core = lax.axis_index("core")
    row_start = tile * rows_dev
    live_slot = jnp.arange(slot_count) < tile_count[0, 0]
    link_flag = live_slot & (tile_rows[0, 0] == column + 1)
    solved = jnp.einsum("sij,jk->sik", cotangent, inverse, preferred_element_type=jnp.float32)
    rounded = jnp.where(
        live_slot[:, None, None], solved.astype(jnp.bfloat16), jnp.zeros_like(cotangent)
    )
    panel_terms = -jnp.einsum("sij,sik->jk", rounded, factors, preferred_element_type=jnp.float32)
    own_rows = lax.dynamic_slice_in_dim(panel_terms, row_start, rows_dev, 0) + diag_cotangent[0]
    panel_terms = lax.dynamic_update_slice_in_dim(panel_terms, own_rows, row_start, 0)
    chosen = jnp.sum(jnp.where(link_flag[:, None, None], factors, jnp.zeros_like(factors)), axis=0)
    link_part = jnp.dot(chosen, inverse, preferred_element_type=jnp.float32)
    mine = all_sum(jnp.concatenate([panel_terms, link_part], axis=0))
    other = swap_cores(mine)
    link_wide = jnp.where(core == 0, other, mine)
    inverse_wide = inverse.astype(jnp.float32)
    lower_wide = lower.astype(jnp.float32)

    def own_of(summed):
        symmetric = symmetrize(jnp.dot(lower_wide.T, summed, precision=chain))
        return 0.5 * jnp.dot(
            inverse_wide.T, jnp.dot(symmetric, inverse_wide, precision=chain), precision=chain
        )

    chain_own = own_of(mine)
    down = [(2 * i, 2 * (i - 1)) for i in range(1, groups)]

    def sweep(_, packed):
        incoming = unpack(packed, width)
        advanced = chain_own + jnp.dot(
            link_wide.T, jnp.dot(incoming, link_wide, precision=chain), precision=chain
        )
        return lax.ppermute(pack(advanced), ("col", "core"), down)

    start = jnp.zeros((BLOCKS * BLOCKS // 2 * width // BLOCKS + 8, width // BLOCKS), jnp.float32)
    packed = lax.fori_loop(0, groups - 1, sweep, start)
    own_map = jnp.where(core == 0, chain_own, lax.ppermute(chain_own, "core", [(0, 1)]))
    shared = lax.ppermute(packed, "core", [(0, 1)])
    incoming = unpack(jnp.where(core == 0, packed, shared), width)
    product = jnp.dot(incoming, link_wide, precision=chain)
    link_rows = lax.dynamic_slice_in_dim(link_wide, row_start, rows_dev, 1)
    own_part = lax.dynamic_slice_in_dim(own_map, row_start, rows_dev, 0)
    diag_rows = own_part + jnp.dot(link_rows.T, product, precision=chain)
    adjusted = (solved - 2.0 * product[None]).astype(jnp.bfloat16)
    panel_out = jnp.where(link_flag[:, None, None], adjusted, rounded)
    return (panel_out[None, None], diag_rows[None])


def solution(mesh):
    cols, tiles = mesh.devices.shape
    split = Mesh(mesh.devices.reshape(cols, tiles // 8, 4, 2), ("col",) + TILE)
    in_specs = (
        P("col", TILE, None, None, None),
        P("col", TILE, None, None, None),
        P("col", None, None),
        P("col", None, None),
        P("col", TILE, None),
        P("col", TILE),
        P("col", TILE, None),
    )
    out_specs = (P("col", TILE, None, None, None), P("col", TILE, None))
    return jax.shard_map(
        on_device, mesh=split, in_specs=in_specs, out_specs=out_specs, check_vma=False
    )
```
